512 devices in a mesh: sk: 32 (over x, y), lang: 16 (over z, core).
Axes of the slice: x: 4, y: 8, z: 8, core: 2. Of those that a mesh axis runs over, the one named last changes fastest.
Arguments:
- embeddings: bfloat16 [524288, 1024], P(('sk', 'lang')), may hold values from -40 to 40
- omega: bfloat16 [524288, 256], P(('sk', 'lang')), may hold values from -0.0078125 to 0.0078125
- lang_ids: int32 [524288, 1], P(('sk', 'lang')), may hold values from 0 to 11; in each aligned block of 1024 rows (0 to 1023, 1024 to 2047, ...) at most 128 rows name the same one
Outputs:
- grouped: bfloat16 [1048576, 256], P(('sk', 'lang'))
The draws below stay inside these ranges and needn't reach their ends.
Inputs may be any that keep to these rules, and one draw needn't show every extreme that they name: `lang_ids`: among the 1024 sentences of one device no language appears more than 128 times, and some language appears exactly 128 times.
All inputs are finite; a program needn't handle non-finite values.
Results may differ from the reference program's by a relative error of at most 0.0075.
Values may be sent and summed in bfloat16 or wider, within the bound.
No kernel may reach another device: no remote copies, remote signals or barrier semaphores. Data moves between devices by JAX's collectives and lax.ppermute only.
A program may use at most 64 MiB of HBM per device.

```python
import math
import jax
import jax.numpy as jnp
import numpy as np
from jax import lax

D = 1024
SKETCH = 256
LANGS = 12
R_DEV = 1024
CAP = 128
ROWS = 524288
N_SK = 32
N_LANG = 16


def draw_embeddings(key, part):
    first_key, second_key = jax.random.split(key, 2)
    fourth_key = jax.random.fold_in(key, 17)
    fifth_key = jax.random.fold_in(key, 23)
    column_scale = jnp.exp(jax.random.uniform(second_key, (D,), jnp.float32, -1.2, 1.2))
    groups = ROWS // R_DEV
    directions = jnp.clip(jax.random.normal(fourth_key, (groups, D), jnp.float32), -4.0, 4.0)
    direction_rows = jnp.repeat(directions, R_DEV, axis=0)
    values = jnp.clip(jax.random.normal(first_key, (ROWS, D), jnp.float32), -5.0, 5.0)
    weights = jnp.clip(jax.random.normal(fifth_key, (ROWS, 1), jnp.float32), -3.0, 3.0)
    mixed = (values + weights * direction_rows) * column_scale[None, :]
    return jnp.clip(mixed, -40.0, 40.0).astype(jnp.bfloat16)


def level_of(rng, extent, cuts, low, top_value):
    def one(dim, parts):
        draws = jax.random.uniform(jax.random.fold_in(jax.random.fold_in(rng, 6), dim), (parts,), jnp.float32, low / len(cuts), top_value / len(cuts))
        return jnp.repeat(jnp.exp(draws), extent[dim] // parts).reshape((-1,) + (1,) * (len(extent) - dim - 1))

    gain = one(*cuts[0])
    for cut in cuts[1:]:
        gain = gain * one(*cut)
    return gain


def assign_block(rng, own, number, rows, count, top, most, slope):
    ranking = jax.random.permutation(rng, count)
    crowded, ordinary = shares(count, rows * top, most, slope, True), shares(count, rows * top, most, slope, False)
    places = jnp.arange(count)

    def named(tallies, offset_by):
        used = int((tallies > 0).sum())
        fixed = max(1, used // 4)
        passed = fixed + (places - fixed + offset_by * (used - fixed)) % max(1, count - fixed)
        return jnp.zeros((count,), jnp.int32).at[ranking[jnp.where(places < fixed, places, passed)]].set(jnp.asarray(tallies, jnp.int32))

    tallies = jnp.where(number % 4 == 0, named(crowded, number // 4), named(ordinary, number - number // 4 - 1))
    mixed = jax.random.permutation(jax.random.fold_in(own, 3), count)
    source_of, receiver = mixed[0:count // 2 * 2:2], mixed[1:count // 2 * 2:2]
    margin = jnp.minimum(tallies[source_of] - 1, most - tallies[receiver]) // 2
    margin = jnp.where((source_of == ranking[0]) | (receiver == ranking[0]) | (tallies[receiver] == 0), 0, jnp.maximum(margin, 0))
    passed = jax.random.randint(jax.random.fold_in(own, 4), (count // 2,), 0, 1 << 20) % (margin + 1)
    tallies = tallies.at[source_of].add(-passed).at[receiver].add(passed)
    labels = jnp.searchsorted(jnp.cumsum(tallies), jnp.arange(rows * top), side="right").astype(jnp.int32)
    grid = labels.reshape(top, rows).T
    grid = grid[jax.random.permutation(jax.random.fold_in(own, 1), rows)]
    offset_by = jax.random.randint(jax.random.fold_in(own, 2), (rows, 1), 0, top)
    return jnp.take_along_axis(grid, (jnp.arange(top)[None, :] + offset_by) % top, axis=1)


def shares(amount, total, reach, lean, full):
    portions = [(1 << 20) // math.isqrt(rank ** lean) + 1 for rank in range(1, amount + 1)]
    largest = reach if full else min(reach, max(-(-total // amount), total * portions[0] // sum(portions)))
    least = 1 if total - largest >= amount - 1 else 0
    holding, surplus = [largest] + [least] * (amount - 1), total - largest - least * (amount - 1)
    while surplus > 0:
        movable = [i for i in range(1, amount) if holding[i] < largest] or [i for i in range(1, amount) if holding[i] < reach]
        mass, left = sum([portions[i] for i in movable]), surplus
        for i in movable:
            addition = min(reach - holding[i], max(1, left * portions[i] // mass), surplus)
            holding[i] = holding[i] + addition
            surplus = surplus - addition
    return np.array(holding)


def normal_values(rng, shape, scale, most, pieces=(), kind=jnp.bfloat16):
    factor_of = level_of(rng, shape, pieces, -0.22, 0.18) if pieces else 1.0
    values = jax.random.normal(rng, shape, jnp.float32) * scale * factor_of
    return jnp.minimum(jnp.maximum(values, -most), most).astype(kind)


def setup_inputs(seed: int = 0) -> dict:
    streams_of = jax.random.split(jax.random.key(seed), 4)
    embeddings = draw_embeddings(jax.random.fold_in(streams_of[3], 71), 0)
    omega = normal_values(streams_of[1], (ROWS, SKETCH), ROWS ** -0.5, 0.0078125, ((0, 512),))
    lang_ids_keys = jax.random.split(jax.random.fold_in(streams_of[2], 1), ROWS // R_DEV)
    lang_ids_turns = jax.random.permutation(jax.random.fold_in(streams_of[2], 3), ROWS // R_DEV)
    lang_ids = jax.vmap(lambda own, number: assign_block(jax.random.fold_in(streams_of[2], 2), own, number, R_DEV, LANGS, 1, CAP, 2))(lang_ids_keys, lang_ids_turns).reshape((ROWS, 1))
    return {"embeddings": embeddings, "omega": omega, "lang_ids": lang_ids}


def orthonormal(sketch):
    gram_matrix = jnp.dot(sketch.astype(jnp.float32), sketch.T.astype(jnp.float32), precision=lax.Precision.HIGHEST, preferred_element_type=jnp.float32)
    lower_factor = jnp.linalg.cholesky(gram_matrix)
    solved = jax.scipy.linalg.solve_triangular(lower_factor, sketch, lower=True)
    return solved.astype(jnp.bfloat16)

def reference(embeddings, omega, lang_ids):
    first_term = jnp.dot(omega.T.astype(jnp.float32), embeddings.astype(jnp.float32), preferred_element_type=jnp.float32)
    first_basis = orthonormal(first_term)
    scores = jnp.dot(embeddings.astype(jnp.float32), first_basis.T.astype(jnp.float32), preferred_element_type=jnp.float32).astype(jnp.bfloat16)
    second_term = jnp.dot(scores.T.astype(jnp.float32), embeddings.astype(jnp.float32), preferred_element_type=jnp.float32)
    second_basis = orthonormal(second_term)
    coords = jnp.dot(embeddings.astype(jnp.float32), second_basis.T.astype(jnp.float32), preferred_element_type=jnp.float32).astype(jnp.bfloat16)
    devices = N_SK * N_LANG
    per_owner = (LANGS + N_LANG - 1) // N_LANG
    languages = lang_ids[:, 0].reshape(devices, R_DEV)
    member = (languages[:, :, None] == jnp.arange(LANGS, dtype=jnp.int32)[None, None, :]).astype(jnp.int32)
    position = jnp.sum(jnp.cumsum(member, axis=1) * member, axis=2) - 1
    target = languages % N_LANG * (per_owner * CAP) + languages // N_LANG * CAP + position
    source = jnp.broadcast_to(jnp.arange(devices, dtype=jnp.int32)[:, None], (devices, R_DEV))
    outgoing = jnp.zeros((devices, N_LANG * per_owner * CAP, SKETCH), jnp.bfloat16)
    outgoing = outgoing.at[source, target].set(coords.reshape(devices, R_DEV, SKETCH))
    outgoing = outgoing.reshape(N_SK, N_LANG, N_LANG, per_owner * CAP, SKETCH)
    outgoing = jnp.transpose(outgoing, (0, 2, 1, 3, 4))
    return outgoing.reshape(devices * N_LANG * per_owner * CAP, SKETCH)
```

```python
import jax
import jax.numpy as jnp
from jax import lax
from jax.sharding import PartitionSpec as P

SKETCH = 256
LANGS = 12
CAP = 128


def all_sum(term):
    axes = ("sk", "lang")
    count = lax.axis_size("sk") * lax.axis_size("lang")
    pieces = term.reshape(count, -1)
    slice_sum = jnp.sum(lax.all_to_all(pieces, axes, 0, 0, tiled=True), axis=0, keepdims=True)
    spread = jnp.broadcast_to(slice_sum, pieces.shape)
    return lax.all_to_all(spread, axes, 0, 0, tiled=True).reshape(term.shape)


def orthonormal(term):
    sketch = all_sum(term)
    gram_matrix = jnp.dot(
        sketch, sketch.T, precision=lax.Precision.HIGHEST, preferred_element_type=jnp.float32
    )
    lower_factor = jnp.linalg.cholesky(gram_matrix)
    return jax.scipy.linalg.solve_triangular(lower_factor, sketch, lower=True).astype(jnp.bfloat16)


def on_device(embeddings, omega, lang_ids):
    first_term = lax.dot_general(
        omega, embeddings, (((0,), (0,)), ((), ())), preferred_element_type=jnp.float32
    )
    first_basis = orthonormal(first_term)
    scores = lax.dot_general(
        embeddings, first_basis, (((1,), (1,)), ((), ())), preferred_element_type=jnp.float32
    ).astype(jnp.bfloat16)
    second_term = lax.dot_general(
        scores, embeddings, (((0,), (0,)), ((), ())), preferred_element_type=jnp.float32
    )
    second_basis = orthonormal(second_term)
    coords = lax.dot_general(
        embeddings, second_basis, (((1,), (1,)), ((), ())), preferred_element_type=jnp.float32
    ).astype(jnp.bfloat16)
    lang_count = lax.axis_size("lang")
    per_owner = (LANGS + lang_count - 1) // lang_count
    languages = lang_ids[:, 0]
    member = (languages[:, None] == jnp.arange(LANGS, dtype=jnp.int32)[None, :]).astype(jnp.int32)
    position = jnp.sum(jnp.cumsum(member, axis=0) * member, axis=1) - 1
    target = languages % lang_count * (per_owner * CAP) + languages // lang_count * CAP + position
    outgoing = (
        jnp.zeros((lang_count * per_owner * CAP, SKETCH), jnp.bfloat16).at[target].set(coords)
    )
    return lax.all_to_all(outgoing, "lang", split_axis=0, concat_axis=0, tiled=True)


def solution(mesh):
    in_specs = (P(("sk", "lang"), None), P(("sk", "lang"), None), P(("sk", "lang"), None))
    out_specs = P(("sk", "lang"), None)
    return jax.shard_map(
        on_device, mesh=mesh, in_specs=in_specs, out_specs=out_specs, check_vma=False
    )
```

```python
import jax
import jax.numpy as jnp
from jax import lax
from jax.experimental import pallas as pl
from jax.experimental.pallas import tpu as pltpu
from jax.sharding import Mesh
from jax.sharding import PartitionSpec as P

SKETCH = 256
LANGS = 12
CAP = 128
PANEL = 32
CORES = 2


def all_sum(term):
    core = lax.axis_index("core")
    rows = term.shape[0] // CORES
    group = lax.axis_size("sk") * lax.axis_size("z")
    pair = [(0, 1), (1, 0)]
    mine = lax.dynamic_slice_in_dim(term, core * rows, rows)
    other = lax.dynamic_slice_in_dim(term, (1 - core) * rows, rows)
    half = mine + lax.ppermute(other, "core", pair)
    pieces = half.reshape(group, -1)
    slice_sum = jnp.sum(lax.all_to_all(pieces, ("sk", "z"), 0, 0, tiled=True), axis=0, keepdims=True)
    spread = jnp.broadcast_to(slice_sum, pieces.shape)
    gathered = lax.all_to_all(spread, ("sk", "z"), 0, 0, tiled=True).reshape(half.shape)
    partner = lax.ppermute(gathered, "core", pair)
    whole = lax.dynamic_update_slice_in_dim(jnp.concatenate([gathered, gathered]), partner, (1 - core) * rows, 0)
    return whole


def eliminate_kernel(g_ref, s_ref, out_ref, a_ref):
    n = g_ref.shape[0]
    width = n + s_ref.shape[1]
    a_ref[:, :n] = g_ref[...]
    a_ref[:, n:] = s_ref[...]
    lane = lax.broadcasted_iota(jnp.int32, (1, width), 1)
    sub = lax.broadcasted_iota(jnp.int32, (PANEL, 1), 0)
    for k in range(0, n, PANEL):
        p = a_ref[k:k + PANEL, :]
        for j in range(PANEL):
            c = k + j
            inv = 1.0 / jnp.sqrt(p[j:j + 1, c:c + 1])
            u = jnp.where(lane >= c, p[j:j + 1, :] * inv, 0.0)
            col = jnp.where(sub > j, p[:, c:c + 1] * inv, 0.0)
            p = jnp.where(sub == j, u, p - col * u)
        out_ref[k:k + PANEL, :] = p[:, n:].astype(out_ref.dtype)
        if k + PANEL < n:
            c0 = ((k + PANEL) // 128) * 128
            update = lax.dot_general(
                p[:, c0:n], p, (((0,), (0,)), ((), ())),
                precision=lax.Precision.HIGHEST, preferred_element_type=jnp.float32)
            a_ref[c0:, :] = a_ref[c0:, :] - update


def orthonormal(term):
    sketch = all_sum(term)
    gram_matrix = jnp.dot(
        sketch, sketch.T, precision=lax.Precision.HIGHEST, preferred_element_type=jnp.float32
    )
    n, m = sketch.shape
    return pl.pallas_call(
        eliminate_kernel,
        out_shape=jax.ShapeDtypeStruct((n, m), jnp.bfloat16),
        in_specs=[pl.BlockSpec(memory_space=pltpu.VMEM)] * 2,
        out_specs=pl.BlockSpec(memory_space=pltpu.VMEM),
        scratch_shapes=[pltpu.VMEM((n, n + m), jnp.float32)],
    )(gram_matrix, sketch)


def on_device(embeddings, omega, lang_ids):
    first_term = lax.dot_general(
        omega, embeddings, (((0,), (0,)), ((), ())), preferred_element_type=jnp.float32
    )
    first_basis = orthonormal(first_term)
    scores = lax.dot_general(
        embeddings, first_basis, (((1,), (1,)), ((), ())), preferred_element_type=jnp.float32
    ).astype(jnp.bfloat16)
    second_term = lax.dot_general(
        scores, embeddings, (((0,), (0,)), ((), ())), preferred_element_type=jnp.float32
    )
    second_basis = orthonormal(second_term)
    coords = lax.dot_general(
        embeddings, second_basis, (((1,), (1,)), ((), ())), preferred_element_type=jnp.float32
    ).astype(jnp.bfloat16)
    lang_count = lax.axis_size("z") * lax.axis_size("core")
    per_owner = (LANGS + lang_count - 1) // lang_count
    languages = lang_ids[:, 0]
    member = (languages[:, None] == jnp.arange(LANGS, dtype=jnp.int32)[None, :]).astype(jnp.int32)
    position = jnp.sum(jnp.cumsum(member, axis=0) * member, axis=1) - 1
    target = languages % lang_count * (per_owner * CAP) + languages // lang_count * CAP + position
    outgoing = (
        jnp.zeros((lang_count * per_owner * CAP, SKETCH), jnp.bfloat16).at[target].set(coords)
    )
    return lax.all_to_all(outgoing, ("z", "core"), split_axis=0, concat_axis=0, tiled=True)


def solution(mesh):
    lang = mesh.shape["lang"]
    split = Mesh(mesh.devices.reshape(mesh.shape["sk"], lang // CORES, CORES), ("sk", "z", "core"))
    spec = P(("sk", "z", "core"), None)
    return jax.shard_map(
        on_device, mesh=split, in_specs=(spec, spec, spec), out_specs=spec, check_vma=False
    )
```

```python
import jax
import jax.numpy as jnp
from jax import lax
from jax.experimental import pallas as pl
from jax.experimental.pallas import tpu as pltpu
from jax.sharding import Mesh
from jax.sharding import PartitionSpec as P

SKETCH = 256
LANGS = 12
CAP = 128
PANEL = 32
CORES = 2


def all_sum(term):
    core = lax.axis_index("core")
    rows = term.shape[0] // CORES
    group = lax.axis_size("sk") * lax.axis_size("z")
    pair = [(0, 1), (1, 0)]
    mine = lax.dynamic_slice_in_dim(term, core * rows, rows)
    other = lax.dynamic_slice_in_dim(term, (1 - core) * rows, rows)
    half = mine + lax.ppermute(other, "core", pair)
    pieces = half.reshape(group, -1)
    slice_sum = jnp.sum(lax.all_to_all(pieces, ("sk", "z"), 0, 0, tiled=True), axis=0, keepdims=True)
    spread = jnp.broadcast_to(slice_sum, pieces.shape)
    gathered = lax.all_to_all(spread, ("sk", "z"), 0, 0, tiled=True).reshape(half.shape)
    partner = lax.ppermute(gathered, "core", pair)
    whole = lax.dynamic_update_slice_in_dim(jnp.concatenate([gathered, gathered]), partner, (1 - core) * rows, 0)
    return whole


def eliminate_kernel(g_ref, s_ref, out_ref, a_ref):
    n = g_ref.shape[0]
    width = n + s_ref.shape[1]
    a_ref[:, :n] = g_ref[...]
    a_ref[:, n:] = s_ref[...]
    sub = lax.broadcasted_iota(jnp.int32, (PANEL, 1), 0)
    diag = lax.broadcasted_iota(jnp.int32, (PANEL, width), 1) - lax.broadcasted_iota(jnp.int32, (PANEL, width), 0)
    for k in range(0, n, PANEL):
        p = a_ref[k:k + PANEL, :]
        scale = jnp.zeros((PANEL, 1), jnp.float32)
        for j in range(PANEL):
            c = k + j
            d = p[j:j + 1, c:c + 1]
            col = jnp.where(sub > j, p[:, c:c + 1] * (1.0 / d), 0.0)
            scale = jnp.where(sub == j, 1.0 / jnp.sqrt(d), scale)
            p = p - col * p[j:j + 1, :]
        p = jnp.where(diag >= k, p * scale, 0.0)
        out_ref[k:k + PANEL, :] = p[:, n:].astype(out_ref.dtype)
        if k + PANEL < n:
            c0 = ((k + PANEL) // 128) * 128
            update = lax.dot_general(
                p[:, c0:n], p, (((0,), (0,)), ((), ())),
                precision=lax.Precision.HIGHEST, preferred_element_type=jnp.float32)
            a_ref[c0:, :] = a_ref[c0:, :] - update


def orthonormal(term):
    sketch = all_sum(term)
    gram_matrix = jnp.dot(
        sketch, sketch.T, precision=lax.Precision.HIGHEST, preferred_element_type=jnp.float32
    )
    n, m = sketch.shape
    return pl.pallas_call(
        eliminate_kernel,
        out_shape=jax.ShapeDtypeStruct((n, m), jnp.bfloat16),
        in_specs=[pl.BlockSpec(memory_space=pltpu.VMEM)] * 2,
        out_specs=pl.BlockSpec(memory_space=pltpu.VMEM),
        scratch_shapes=[pltpu.VMEM((n, n + m), jnp.float32)],
    )(gram_matrix, sketch)


def on_device(embeddings, omega, lang_ids):
    first_term = lax.dot_general(
        omega, embeddings, (((0,), (0,)), ((), ())), preferred_element_type=jnp.float32
    )
    first_basis = orthonormal(first_term)
    scores = lax.dot_general(
        embeddings, first_basis, (((1,), (1,)), ((), ())), preferred_element_type=jnp.float32
    ).astype(jnp.bfloat16)
    second_term = lax.dot_general(
        scores, embeddings, (((0,), (0,)), ((), ())), preferred_element_type=jnp.float32
    )
    second_basis = orthonormal(second_term)
    coords = lax.dot_general(
        embeddings, second_basis, (((1,), (1,)), ((), ())), preferred_element_type=jnp.float32
    ).astype(jnp.bfloat16)
    lang_count = lax.axis_size("z") * lax.axis_size("core")
    per_owner = (LANGS + lang_count - 1) // lang_count
    languages = lang_ids[:, 0]
    member = (languages[:, None] == jnp.arange(LANGS, dtype=jnp.int32)[None, :]).astype(jnp.int32)
    position = jnp.sum(jnp.cumsum(member, axis=0) * member, axis=1) - 1
    target = languages % lang_count * (per_owner * CAP) + languages // lang_count * CAP + position
    outgoing = (
        jnp.zeros((lang_count * per_owner * CAP, SKETCH), jnp.bfloat16).at[target].set(coords)
    )
    return lax.all_to_all(outgoing, ("z", "core"), split_axis=0, concat_axis=0, tiled=True)


def solution(mesh):
    lang = mesh.shape["lang"]
    split = Mesh(mesh.devices.reshape(mesh.shape["sk"], lang // CORES, CORES), ("sk", "z", "core"))
    spec = P(("sk", "z", "core"), None)
    return jax.shard_map(
        on_device, mesh=split, in_specs=(spec, spec, spec), out_specs=spec, check_vma=False
    )
```

```python
import jax
import jax.numpy as jnp
from jax import lax
from jax.experimental import pallas as pl
from jax.experimental.pallas import tpu as pltpu
from jax.sharding import Mesh
from jax.sharding import PartitionSpec as P

SKETCH = 256
LANGS = 12
CAP = 128
PANEL = 32
CORES = 2


def all_sum(term):
    core = lax.axis_index("core")
    rows = term.shape[0] // CORES
    group = lax.axis_size("sk") * lax.axis_size("z")
    pair = [(0, 1), (1, 0)]
    mine = lax.dynamic_slice_in_dim(term, core * rows, rows)
    other = lax.dynamic_slice_in_dim(term, (1 - core) * rows, rows)
    half = mine + lax.ppermute(other, "core", pair)
    pieces = half.reshape(group, -1)
    slice_sum = jnp.sum(lax.all_to_all(pieces, ("sk", "z"), 0, 0, tiled=True), axis=0, keepdims=True)
    spread = jnp.broadcast_to(slice_sum, pieces.shape)
    gathered = lax.all_to_all(spread, ("sk", "z"), 0, 0, tiled=True).reshape(half.shape)
    partner = lax.ppermute(gathered, "core", pair)
    whole = lax.dynamic_update_slice_in_dim(jnp.concatenate([gathered, gathered]), partner, (1 - core) * rows, 0)
    return whole


def eliminate_kernel(g_ref, s_ref, out_ref, a_ref):
    n = g_ref.shape[0]
    width = n + s_ref.shape[1]
    a_ref[:, :n] = g_ref[...]
    a_ref[:, n:] = s_ref[...]
    sub = lax.broadcasted_iota(jnp.int32, (PANEL, 1), 0)
    diag = lax.broadcasted_iota(jnp.int32, (PANEL, width), 1) - lax.broadcasted_iota(jnp.int32, (PANEL, width), 0)
    for k in range(0, n, PANEL):
        p = a_ref[k:k + PANEL, :]
        scale = jnp.zeros((PANEL, 1), jnp.float32)
        for j in range(PANEL):
            c = k + j
            d = p[j:j + 1, c:c + 1]
            col = jnp.where(sub > j, p[:, c:c + 1] * (1.0 / d), 0.0)
            scale = jnp.where(sub == j, 1.0 / jnp.sqrt(d), scale)
            p = p - col * p[j:j + 1, :]
        p = jnp.where(diag >= k, p * scale, 0.0)
        out_ref[k:k + PANEL, :] = p[:, n:].astype(out_ref.dtype)
        if k + PANEL < n:
            c0 = ((k + PANEL) // 128) * 128
            update = lax.dot_general(
                p[:, c0:n], p, (((0,), (0,)), ((), ())),
                precision=lax.Precision.HIGHEST, preferred_element_type=jnp.float32)
            a_ref[c0:, :] = a_ref[c0:, :] - update


def orthonormal(term):
    sketch = all_sum(term)
    gram_matrix = jnp.dot(
        sketch, sketch.T, precision=lax.Precision.HIGHEST, preferred_element_type=jnp.float32
    )
    n, m = sketch.shape
    return pl.pallas_call(
        eliminate_kernel,
        out_shape=jax.ShapeDtypeStruct((n, m), jnp.bfloat16),
        in_specs=[pl.BlockSpec(memory_space=pltpu.VMEM)] * 2,
        out_specs=pl.BlockSpec(memory_space=pltpu.VMEM),
        scratch_shapes=[pltpu.VMEM((n, n + m), jnp.float32)],
    )(gram_matrix, sketch)


def on_device(embeddings, omega, lang_ids):
    first_term = lax.dot_general(
        omega, embeddings, (((0,), (0,)), ((), ())), preferred_element_type=jnp.float32
    )
    first_basis = orthonormal(first_term)
    scores = lax.dot_general(
        embeddings, first_basis, (((1,), (1,)), ((), ())), preferred_element_type=jnp.float32
    ).astype(jnp.bfloat16)
    second_term = lax.dot_general(
        scores, embeddings, (((0,), (0,)), ((), ())), preferred_element_type=jnp.float32
    )
    second_basis = orthonormal(second_term)
    coords = lax.dot_general(
        embeddings, second_basis, (((1,), (1,)), ((), ())), preferred_element_type=jnp.float32
    ).astype(jnp.bfloat16)
    lang_count = lax.axis_size("z") * lax.axis_size("core")
    per_owner = (LANGS + lang_count - 1) // lang_count
    languages = lang_ids[:, 0]
    member = (languages[:, None] == jnp.arange(LANGS, dtype=jnp.int32)[None, :]).astype(jnp.int32)
    position = jnp.sum(jnp.cumsum(member, axis=0) * member, axis=1) - 1
    target = languages % lang_count * (per_owner * CAP) + languages // lang_count * CAP + position
    slots = lax.broadcasted_iota(jnp.int32, (lang_count * per_owner * CAP, 1), 0)
    chooser = (slots == target[None, :]).astype(jnp.bfloat16)
    outgoing = jnp.dot(chooser, coords, preferred_element_type=jnp.float32).astype(jnp.bfloat16)
    return lax.all_to_all(outgoing, ("z", "core"), split_axis=0, concat_axis=0, tiled=True)


def solution(mesh):
    lang = mesh.shape["lang"]
    split = Mesh(mesh.devices.reshape(mesh.shape["sk"], lang // CORES, CORES), ("sk", "z", "core"))
    spec = P(("sk", "z", "core"), None)
    return jax.shard_map(
        on_device, mesh=split, in_specs=(spec, spec, spec), out_specs=spec, check_vma=False
    )
```

```python
import jax
import jax.numpy as jnp
from jax import lax
from jax.experimental import pallas as pl
from jax.experimental.pallas import tpu as pltpu
from jax.sharding import Mesh
from jax.sharding import PartitionSpec as P

SKETCH = 256
LANGS = 12
CAP = 128
PANEL = 32
CORES = 2


def all_sum(term):
    core = lax.axis_index("core")
    rows = term.shape[0] // CORES
    group = lax.axis_size("sk") * lax.axis_size("z")
    pair = [(0, 1), (1, 0)]
    mine = lax.dynamic_slice_in_dim(term, core * rows, rows)
    other = lax.dynamic_slice_in_dim(term, (1 - core) * rows, rows)
    half = mine + lax.ppermute(other, "core", pair)
    pieces = half.reshape(group, -1)
    slice_sum = jnp.sum(lax.all_to_all(pieces, ("sk", "z"), 0, 0, tiled=True), axis=0, keepdims=True)
    spread = jnp.broadcast_to(slice_sum, pieces.shape)
    gathered = lax.all_to_all(spread, ("sk", "z"), 0, 0, tiled=True).reshape(half.shape)
    partner = lax.ppermute(gathered, "core", pair)
    whole = lax.dynamic_update_slice_in_dim(jnp.concatenate([gathered, gathered]), partner, (1 - core) * rows, 0)
    return whole


def eliminate_kernel(g_ref, s_ref, out_ref, a_ref):
    n = g_ref.shape[0]
    width = n + s_ref.shape[1]
    a_ref[:, :n] = g_ref[...]
    a_ref[:, n:] = s_ref[...]
    sub = lax.broadcasted_iota(jnp.int32, (PANEL, 1), 0)
    diag = lax.broadcasted_iota(jnp.int32, (PANEL, width), 1) - lax.broadcasted_iota(jnp.int32, (PANEL, width), 0)
    for k in range(0, n, PANEL):
        p = a_ref[k:k + PANEL, :]
        scale = jnp.zeros((PANEL, 1), jnp.float32)
        for j in range(PANEL):
            c = k + j
            d = p[j:j + 1, c:c + 1]
            col = jnp.where(sub > j, p[:, c:c + 1] * (1.0 / d), 0.0)
            scale = jnp.where(sub == j, 1.0 / jnp.sqrt(d), scale)
            p = p - col * p[j:j + 1, :]
        p = jnp.where(diag >= k, p * scale, 0.0)
        out_ref[k:k + PANEL, :] = p[:, n:].astype(out_ref.dtype)
        if k + PANEL < n:
            c0 = ((k + PANEL) // 128) * 128
            update = lax.dot_general(
                p[:, c0:n], p, (((0,), (0,)), ((), ())),
                precision=lax.Precision.HIGHEST, preferred_element_type=jnp.float32)
            a_ref[c0:, :] = a_ref[c0:, :] - update


def orthonormal(term):
    sketch = all_sum(term)
    gram_matrix = jnp.dot(
        sketch, sketch.T, precision=lax.Precision.HIGHEST, preferred_element_type=jnp.float32
    )
    n, m = sketch.shape
    return pl.pallas_call(
        eliminate_kernel,
        out_shape=jax.ShapeDtypeStruct((n, m), jnp.bfloat16),
        in_specs=[pl.BlockSpec(memory_space=pltpu.VMEM)] * 2,
        out_specs=pl.BlockSpec(memory_space=pltpu.VMEM),
        scratch_shapes=[pltpu.VMEM((n, n + m), jnp.float32)],
    )(gram_matrix, sketch)


def on_device(embeddings, omega, lang_ids):
    def power_step(_, carry):
        term, _ = carry
        basis = orthonormal(term)
        scores = lax.dot_general(
            embeddings, basis, (((1,), (1,)), ((), ())), preferred_element_type=jnp.float32
        ).astype(jnp.bfloat16)
        following = lax.dot_general(
            scores, embeddings, (((0,), (0,)), ((), ())), preferred_element_type=jnp.float32
        )
        return following, basis

    first_term = lax.dot_general(
        omega, embeddings, (((0,), (0,)), ((), ())), preferred_element_type=jnp.float32
    )
    start = (first_term, jnp.zeros(first_term.shape, jnp.bfloat16))
    _, second_basis = lax.fori_loop(0, 2, power_step, start)
    coords = lax.dot_general(
        embeddings, second_basis, (((1,), (1,)), ((), ())), preferred_element_type=jnp.float32
    ).astype(jnp.bfloat16)
    lang_count = lax.axis_size("z") * lax.axis_size("core")
    per_owner = (LANGS + lang_count - 1) // lang_count
    languages = lang_ids[:, 0]
    member = (languages[:, None] == jnp.arange(LANGS, dtype=jnp.int32)[None, :]).astype(jnp.int32)
    position = jnp.sum(jnp.cumsum(member, axis=0) * member, axis=1) - 1
    target = languages % lang_count * (per_owner * CAP) + languages // lang_count * CAP + position
    slots = lax.broadcasted_iota(jnp.int32, (lang_count * per_owner * CAP, 1), 0)
    chooser = (slots == target[None, :]).astype(jnp.bfloat16)
    outgoing = jnp.dot(chooser, coords, preferred_element_type=jnp.float32).astype(jnp.bfloat16)
    return lax.all_to_all(outgoing, ("z", "core"), split_axis=0, concat_axis=0, tiled=True)


def solution(mesh):
    lang = mesh.shape["lang"]
    split = Mesh(mesh.devices.reshape(mesh.shape["sk"], lang // CORES, CORES), ("sk", "z", "core"))
    spec = P(("sk", "z", "core"), None)
    return jax.shard_map(
        on_device, mesh=split, in_specs=(spec, spec, spec), out_specs=spec, check_vma=False
    )
```

```python
import jax
import jax.numpy as jnp
from jax import lax
from jax.experimental import pallas as pl
from jax.experimental.pallas import tpu as pltpu
from jax.sharding import Mesh
from jax.sharding import PartitionSpec as P

SKETCH = 256
LANGS = 12
CAP = 128
PANEL = 32
CORES = 2


def all_sum(term):
    core = lax.axis_index("core")
    rows = term.shape[0] // CORES
    group = lax.axis_size("sk") * lax.axis_size("z")
    pair = [(0, 1), (1, 0)]
    mine = lax.dynamic_slice_in_dim(term, core * rows, rows)
    other = lax.dynamic_slice_in_dim(term, (1 - core) * rows, rows)
    half = mine + lax.ppermute(other, "core", pair)
    pieces = half.reshape(group, -1)
    slice_sum = jnp.sum(lax.all_to_all(pieces, ("sk", "z"), 0, 0, tiled=True), axis=0, keepdims=True)
    spread = jnp.broadcast_to(slice_sum, pieces.shape)
    gathered = lax.all_to_all(spread, ("sk", "z"), 0, 0, tiled=True).reshape(half.shape)
    partner = lax.ppermute(gathered, "core", pair)
    whole = lax.dynamic_update_slice_in_dim(jnp.concatenate([gathered, gathered]), partner, (1 - core) * rows, 0)
    return whole


def eliminate_kernel(g_ref, s_ref, out_ref, a_ref):
    n = g_ref.shape[0]
    width = n + s_ref.shape[1]
    a_ref[:, :n] = g_ref[...]
    a_ref[:, n:] = s_ref[...]
    sub = lax.broadcasted_iota(jnp.int32, (PANEL, 1), 0)
    diag = lax.broadcasted_iota(jnp.int32, (PANEL, width), 1) - lax.broadcasted_iota(jnp.int32, (PANEL, width), 0)
    for k in range(0, n, PANEL):
        p = a_ref[k:k + PANEL, :]
        scale = jnp.zeros((PANEL, 1), jnp.float32)
        for j in range(PANEL):
            c = k + j
            d = p[j:j + 1, c:c + 1]
            col = jnp.where(sub > j, p[:, c:c + 1] * (1.0 / d), 0.0)
            scale = jnp.where(sub == j, 1.0 / jnp.sqrt(d), scale)
            p = p - col * p[j:j + 1, :]
        p = jnp.where(diag >= k, p * scale, 0.0)
        out_ref[k:k + PANEL, :] = p[:, n:].astype(out_ref.dtype)
        if k + PANEL < n:
            c0 = ((k + PANEL) // 128) * 128
            update = lax.dot_general(
                p[:, c0:n], p, (((0,), (0,)), ((), ())),
                precision=lax.Precision.HIGHEST, preferred_element_type=jnp.float32)
            a_ref[c0:, :] = a_ref[c0:, :] - update


def orthonormal(term):
    sketch = all_sum(term)
    gram_matrix = jnp.dot(
        sketch, sketch.T, precision=lax.Precision.HIGHEST, preferred_element_type=jnp.float32
    )
    n, m = sketch.shape
    return pl.pallas_call(
        eliminate_kernel,
        out_shape=jax.ShapeDtypeStruct((n, m), jnp.bfloat16),
        in_specs=[pl.BlockSpec(memory_space=pltpu.VMEM)] * 2,
        out_specs=pl.BlockSpec(memory_space=pltpu.VMEM),
        scratch_shapes=[pltpu.VMEM((n, n + m), jnp.float32)],
    )(gram_matrix, sketch)


def on_device(embeddings, omega, lang_ids):
    def power_step(_, carry):
        term, _ = carry
        basis = orthonormal(term)
        scores = lax.dot_general(
            embeddings, basis, (((1,), (1,)), ((), ())), preferred_element_type=jnp.float32
        ).astype(jnp.bfloat16)
        following = lax.dot_general(
            scores, embeddings, (((0,), (0,)), ((), ())), preferred_element_type=jnp.float32
        )
        return following, basis

    first_term = lax.dot_general(
        omega, embeddings, (((0,), (0,)), ((), ())), preferred_element_type=jnp.float32
    )
    start = (first_term, jnp.zeros(first_term.shape, jnp.bfloat16))
    _, second_basis = lax.fori_loop(0, 2, power_step, start)
    coords = lax.dot_general(
        embeddings, second_basis, (((1,), (1,)), ((), ())), preferred_element_type=jnp.float32
    ).astype(jnp.bfloat16)
    lang_count = lax.axis_size("z") * lax.axis_size("core")
    per_owner = (LANGS + lang_count - 1) // lang_count
    languages = lang_ids[:, 0]
    member = (languages[:, None] == jnp.arange(LANGS, dtype=jnp.int32)[None, :]).astype(jnp.bfloat16)
    rows = languages.shape[0]
    earlier = (
        lax.broadcasted_iota(jnp.int32, (rows, rows), 0) > lax.broadcasted_iota(jnp.int32, (rows, rows), 1)
    ).astype(jnp.bfloat16)
    counts = jnp.dot(earlier, member, preferred_element_type=jnp.float32)
    position = jnp.sum(counts * member.astype(jnp.float32), axis=1).astype(jnp.int32)
    target = languages % lang_count * (per_owner * CAP) + languages // lang_count * CAP + position
    slots = lax.broadcasted_iota(jnp.int32, (lang_count * per_owner * CAP, 1), 0)
    chooser = (slots == target[None, :]).astype(jnp.bfloat16)
    outgoing = jnp.dot(chooser, coords, preferred_element_type=jnp.float32).astype(jnp.bfloat16)
    return lax.all_to_all(outgoing, ("z", "core"), split_axis=0, concat_axis=0, tiled=True)


def solution(mesh):
    lang = mesh.shape["lang"]
    split = Mesh(mesh.devices.reshape(mesh.shape["sk"], lang // CORES, CORES), ("sk", "z", "core"))
    spec = P(("sk", "z", "core"), None)
    return jax.shard_map(
        on_device, mesh=split, in_specs=(spec, spec, spec), out_specs=spec, check_vma=False
    )
```

```python
import jax
import jax.numpy as jnp
from jax import lax
from jax.experimental import pallas as pl
from jax.experimental.pallas import tpu as pltpu
from jax.sharding import Mesh
from jax.sharding import PartitionSpec as P

SKETCH = 256
LANGS = 12
CAP = 128
PANEL = 32
CORES = 2


def all_sum(term):
    core = lax.axis_index("core")
    rows = term.shape[0] // CORES
    group = lax.axis_size("sk") * lax.axis_size("z")
    pair = [(0, 1), (1, 0)]
    mine = lax.dynamic_slice_in_dim(term, core * rows, rows)
    other = lax.dynamic_slice_in_dim(term, (1 - core) * rows, rows)
    half = mine + lax.ppermute(other, "core", pair)
    pieces = half.reshape(group, -1)
    slice_sum = jnp.sum(lax.all_to_all(pieces, ("sk", "z"), 0, 0, tiled=True), axis=0, keepdims=True)
    spread = jnp.broadcast_to(slice_sum, pieces.shape)
    gathered = lax.all_to_all(spread, ("sk", "z"), 0, 0, tiled=True).reshape(half.shape)
    partner = lax.ppermute(gathered, "core", pair)
    whole = lax.dynamic_update_slice_in_dim(jnp.concatenate([gathered, gathered]), partner, (1 - core) * rows, 0)
    return whole


def eliminate_kernel(g_ref, s_ref, out_ref, a_ref):
    n = g_ref.shape[0]
    width = n + s_ref.shape[1]
    a_ref[:, :n] = g_ref[...]
    a_ref[:, n:] = s_ref[...]
    sub = lax.broadcasted_iota(jnp.int32, (PANEL, 1), 0)
    diag = lax.broadcasted_iota(jnp.int32, (PANEL, width), 1) - lax.broadcasted_iota(jnp.int32, (PANEL, width), 0)
    for k in range(0, n, PANEL):
        p = a_ref[k:k + PANEL, :]
        scale = jnp.zeros((PANEL, 1), jnp.float32)
        for j in range(PANEL):
            c = k + j
            d = p[j:j + 1, c:c + 1]
            col = jnp.where(sub > j, p[:, c:c + 1] * (1.0 / d), 0.0)
            scale = jnp.where(sub == j, 1.0 / jnp.sqrt(d), scale)
            p = p - col * p[j:j + 1, :]
        p = jnp.where(diag >= k, p * scale, 0.0)
        out_ref[k:k + PANEL, :] = p[:, n:].astype(out_ref.dtype)
        if k + PANEL < n:
            c0 = ((k + PANEL) // 128) * 128
            update = lax.dot_general(
                p[:, c0:n], p, (((0,), (0,)), ((), ())),
                precision=lax.Precision.HIGHEST, preferred_element_type=jnp.float32)
            a_ref[c0:, :] = a_ref[c0:, :] - update


def orthonormal(term):
    sketch = all_sum(term)
    gram_matrix = jnp.dot(
        sketch, sketch.T, precision=lax.Precision.HIGHEST, preferred_element_type=jnp.float32
    )
    n, m = sketch.shape
    return pl.pallas_call(
        eliminate_kernel,
        out_shape=jax.ShapeDtypeStruct((n, m), jnp.bfloat16),
        in_specs=[pl.BlockSpec(memory_space=pltpu.VMEM)] * 2,
        out_specs=pl.BlockSpec(memory_space=pltpu.VMEM),
        scratch_shapes=[pltpu.VMEM((n, n + m), jnp.float32)],
    )(gram_matrix, sketch)


def on_device(embeddings, omega, lang_ids):
    def power_step(_, carry):
        term, _ = carry
        basis = orthonormal(term)
        scores = lax.dot_general(
            embeddings, basis, (((1,), (1,)), ((), ())), preferred_element_type=jnp.float32
        ).astype(jnp.bfloat16)
        following = lax.dot_general(
            scores, embeddings, (((0,), (0,)), ((), ())), preferred_element_type=jnp.float32
        )
        return following, scores

    first_term = lax.dot_general(
        omega, embeddings, (((0,), (0,)), ((), ())), preferred_element_type=jnp.float32
    )
    start = (first_term, jnp.zeros((embeddings.shape[0], SKETCH), jnp.bfloat16))
    _, coords = lax.fori_loop(0, 2, power_step, start)
    lang_count = lax.axis_size("z") * lax.axis_size("core")
    per_owner = (LANGS + lang_count - 1) // lang_count
    languages = lang_ids[:, 0]
    member = (languages[:, None] == jnp.arange(LANGS, dtype=jnp.int32)[None, :]).astype(jnp.bfloat16)
    rows = languages.shape[0]
    earlier = (
        lax.broadcasted_iota(jnp.int32, (rows, rows), 0) > lax.broadcasted_iota(jnp.int32, (rows, rows), 1)
    ).astype(jnp.bfloat16)
    counts = jnp.dot(earlier, member, preferred_element_type=jnp.float32)
    position = jnp.sum(counts * member.astype(jnp.float32), axis=1).astype(jnp.int32)
    target = languages % lang_count * (per_owner * CAP) + languages // lang_count * CAP + position
    slots = lax.broadcasted_iota(jnp.int32, (lang_count * per_owner * CAP, 1), 0)
    chooser = (slots == target[None, :]).astype(jnp.bfloat16)
    outgoing = jnp.dot(chooser, coords, preferred_element_type=jnp.float32).astype(jnp.bfloat16)
    return lax.all_to_all(outgoing, ("z", "core"), split_axis=0, concat_axis=0, tiled=True)


def solution(mesh):
    lang = mesh.shape["lang"]
    split = Mesh(mesh.devices.reshape(mesh.shape["sk"], lang // CORES, CORES), ("sk", "z", "core"))
    spec = P(("sk", "z", "core"), None)
    return jax.shard_map(
        on_device, mesh=split, in_specs=(spec, spec, spec), out_specs=spec, check_vma=False
    )
```

```python
import jax
import jax.numpy as jnp
from jax import lax
from jax.experimental import pallas as pl
from jax.experimental.pallas import tpu as pltpu
from jax.sharding import Mesh
from jax.sharding import PartitionSpec as P

SKETCH = 256
LANGS = 12
CAP = 128
PANEL = 32
CORES = 2


def all_sum(term):
    core = lax.axis_index("core")
    rows = term.shape[0] // CORES
    group = lax.axis_size("sk") * lax.axis_size("z")
    pair = [(0, 1), (1, 0)]
    mine = lax.dynamic_slice_in_dim(term, core * rows, rows)
    other = lax.dynamic_slice_in_dim(term, (1 - core) * rows, rows)
    half = mine + lax.ppermute(other, "core", pair)
    pieces = half.reshape(group, -1)
    slice_sum = jnp.sum(lax.all_to_all(pieces, ("sk", "z"), 0, 0, tiled=True), axis=0, keepdims=True)
    spread = jnp.broadcast_to(slice_sum, pieces.shape)
    gathered = lax.all_to_all(spread, ("sk", "z"), 0, 0, tiled=True).reshape(half.shape)
    partner = lax.ppermute(gathered, "core", pair)
    whole = lax.dynamic_update_slice_in_dim(jnp.concatenate([gathered, gathered]), partner, (1 - core) * rows, 0)
    return whole


def eliminate_kernel(s_ref, out_ref, a_ref):
    n = s_ref.shape[0]
    width = n + s_ref.shape[1]
    a_ref[:, n:] = s_ref[...]
    a_ref[:, :n] = lax.dot_general(
        s_ref[...], s_ref[...], (((1,), (1,)), ((), ())),
        precision=lax.Precision.HIGHEST, preferred_element_type=jnp.float32)
    sub = lax.broadcasted_iota(jnp.int32, (PANEL, 1), 0)
    diag = lax.broadcasted_iota(jnp.int32, (PANEL, width), 1) - lax.broadcasted_iota(jnp.int32, (PANEL, width), 0)
    for k in range(0, n, PANEL):
        p = a_ref[k:k + PANEL, :]
        scale = jnp.zeros((PANEL, 1), jnp.float32)
        for j in range(PANEL):
            c = k + j
            d = p[j:j + 1, c:c + 1]
            col = jnp.where(sub > j, p[:, c:c + 1] * (1.0 / d), 0.0)
            scale = jnp.where(sub == j, 1.0 / jnp.sqrt(d), scale)
            p = p - col * p[j:j + 1, :]
        p = jnp.where(diag >= k, p * scale, 0.0)
        out_ref[k:k + PANEL, :] = p[:, n:].astype(out_ref.dtype)
        if k + PANEL < n:
            c0 = ((k + PANEL) // 128) * 128
            update = lax.dot_general(
                p[:, c0:n], p, (((0,), (0,)), ((), ())),
                precision=lax.Precision.HIGHEST, preferred_element_type=jnp.float32)
            a_ref[c0:, :] = a_ref[c0:, :] - update


def orthonormal(term):
    sketch = all_sum(term)
    n, m = sketch.shape
    return pl.pallas_call(
        eliminate_kernel,
        out_shape=jax.ShapeDtypeStruct((n, m), jnp.bfloat16),
        in_specs=[pl.BlockSpec(memory_space=pltpu.VMEM)],
        out_specs=pl.BlockSpec(memory_space=pltpu.VMEM),
        scratch_shapes=[pltpu.VMEM((n, n + m), jnp.float32)],
    )(sketch)


def on_device(embeddings, omega, lang_ids):
    def power_step(_, carry):
        term, _ = carry
        basis = orthonormal(term)
        scores = lax.dot_general(
            embeddings, basis, (((1,), (1,)), ((), ())), preferred_element_type=jnp.float32
        ).astype(jnp.bfloat16)
        following = lax.dot_general(
            scores, embeddings, (((0,), (0,)), ((), ())), preferred_element_type=jnp.float32
        )
        return following, basis

    first_term = lax.dot_general(
        omega, embeddings, (((0,), (0,)), ((), ())), preferred_element_type=jnp.float32
    )
    start = (first_term, jnp.zeros(first_term.shape, jnp.bfloat16))
    _, second_basis = lax.fori_loop(0, 2, power_step, start)
    coords = lax.dot_general(
        embeddings, second_basis, (((1,), (1,)), ((), ())), preferred_element_type=jnp.float32
    ).astype(jnp.bfloat16)
    lang_count = lax.axis_size("z") * lax.axis_size("core")
    per_owner = (LANGS + lang_count - 1) // lang_count
    languages = lang_ids[:, 0]
    member = (languages[:, None] == jnp.arange(LANGS, dtype=jnp.int32)[None, :]).astype(jnp.bfloat16)
    rows = languages.shape[0]
    earlier = (
        lax.broadcasted_iota(jnp.int32, (rows, rows), 0) > lax.broadcasted_iota(jnp.int32, (rows, rows), 1)
    ).astype(jnp.bfloat16)
    counts = jnp.dot(earlier, member, preferred_element_type=jnp.float32)
    position = jnp.sum(counts * member.astype(jnp.float32), axis=1).astype(jnp.int32)
    target = languages % lang_count * (per_owner * CAP) + languages // lang_count * CAP + position
    slots = lax.broadcasted_iota(jnp.int32, (lang_count * per_owner * CAP, 1), 0)
    chooser = (slots == target[None, :]).astype(jnp.bfloat16)
    outgoing = jnp.dot(chooser, coords, preferred_element_type=jnp.float32).astype(jnp.bfloat16)
    return lax.all_to_all(outgoing, ("z", "core"), split_axis=0, concat_axis=0, tiled=True)


def solution(mesh):
    lang = mesh.shape["lang"]
    split = Mesh(mesh.devices.reshape(mesh.shape["sk"], lang // CORES, CORES), ("sk", "z", "core"))
    spec = P(("sk", "z", "core"), None)
    return jax.shard_map(
        on_device, mesh=split, in_specs=(spec, spec, spec), out_specs=spec, check_vma=False
    )
```

```python
import jax
import jax.numpy as jnp
from jax import lax
from jax.experimental import pallas as pl
from jax.experimental.pallas import tpu as pltpu
from jax.sharding import Mesh
from jax.sharding import PartitionSpec as P

SKETCH = 256
LANGS = 12
CAP = 128
PANEL = 32
CORES = 2


def term_halves(weights, embeddings):
    core = lax.axis_index("core")
    rows = weights.shape[1] // CORES
    dims = (((0,), (0,)), ((), ()))
    other = lax.dot_general(lax.dynamic_slice_in_dim(weights, (1 - core) * rows, rows, axis=1), embeddings, dims,
                            preferred_element_type=jnp.float32)
    mine = lax.dot_general(lax.dynamic_slice_in_dim(weights, core * rows, rows, axis=1), embeddings, dims,
                           preferred_element_type=jnp.float32)
    return mine, other


def all_sum(mine, other):
    core = lax.axis_index("core")
    rows = mine.shape[0]
    group = lax.axis_size("sk") * lax.axis_size("z")
    pair = [(0, 1), (1, 0)]
    half = mine + lax.ppermute(other, "core", pair)
    pieces = half.reshape(group, -1)
    slice_sum = jnp.sum(lax.all_to_all(pieces, ("sk", "z"), 0, 0, tiled=True), axis=0, keepdims=True)
    spread = jnp.broadcast_to(slice_sum, pieces.shape)
    gathered = lax.all_to_all(spread, ("sk", "z"), 0, 0, tiled=True).reshape(half.shape)
    partner = lax.ppermute(gathered, "core", pair)
    whole = lax.dynamic_update_slice_in_dim(jnp.concatenate([gathered, gathered]), partner, (1 - core) * rows, 0)
    return whole


def eliminate_kernel(g_ref, s_ref, out_ref, a_ref):
    n = g_ref.shape[0]
    width = n + s_ref.shape[1]
    a_ref[:, :n] = g_ref[...]
    a_ref[:, n:] = s_ref[...]
    sub = lax.broadcasted_iota(jnp.int32, (PANEL, 1), 0)
    diag = lax.broadcasted_iota(jnp.int32, (PANEL, width), 1) - lax.broadcasted_iota(jnp.int32, (PANEL, width), 0)
    for k in range(0, n, PANEL):
        p = a_ref[k:k + PANEL, :]
        scale = jnp.zeros((PANEL, 1), jnp.float32)
        for j in range(PANEL):
            c = k + j
            d = p[j:j + 1, c:c + 1]
            col = jnp.where(sub > j, p[:, c:c + 1] * (1.0 / d), 0.0)
            scale = jnp.where(sub == j, 1.0 / jnp.sqrt(d), scale)
            p = p - col * p[j:j + 1, :]
        p = jnp.where(diag >= k, p * scale, 0.0)
        out_ref[k:k + PANEL, :] = p[:, n:].astype(out_ref.dtype)
        if k + PANEL < n:
            c0 = ((k + PANEL) // 128) * 128
            update = lax.dot_general(
                p[:, c0:n], p, (((0,), (0,)), ((), ())),
                precision=lax.Precision.HIGHEST, preferred_element_type=jnp.float32)
            a_ref[c0:, :] = a_ref[c0:, :] - update


def orthonormal(mine, other):
    sketch = all_sum(mine, other)
    gram_matrix = jnp.dot(
        sketch, sketch.T, precision=lax.Precision.HIGHEST, preferred_element_type=jnp.float32
    )
    n, m = sketch.shape
    return pl.pallas_call(
        eliminate_kernel,
        out_shape=jax.ShapeDtypeStruct((n, m), jnp.bfloat16),
        in_specs=[pl.BlockSpec(memory_space=pltpu.VMEM)] * 2,
        out_specs=pl.BlockSpec(memory_space=pltpu.VMEM),
        scratch_shapes=[pltpu.VMEM((n, n + m), jnp.float32)],
    )(gram_matrix, sketch)


def on_device(embeddings, omega, lang_ids):
    def power_step(_, carry):
        mine, other, _ = carry
        basis = orthonormal(mine, other)
        scores = lax.dot_general(
            embeddings, basis, (((1,), (1,)), ((), ())), preferred_element_type=jnp.float32
        ).astype(jnp.bfloat16)
        return term_halves(scores, embeddings) + (basis,)

    start = term_halves(omega, embeddings) + (jnp.zeros((SKETCH, embeddings.shape[1]), jnp.bfloat16),)
    _, _, second_basis = lax.fori_loop(0, 2, power_step, start)
    coords = lax.dot_general(
        embeddings, second_basis, (((1,), (1,)), ((), ())), preferred_element_type=jnp.float32
    ).astype(jnp.bfloat16)
    lang_count = lax.axis_size("z") * lax.axis_size("core")
    per_owner = (LANGS + lang_count - 1) // lang_count
    languages = lang_ids[:, 0]
    member = (languages[:, None] == jnp.arange(LANGS, dtype=jnp.int32)[None, :]).astype(jnp.bfloat16)
    rows = languages.shape[0]
    earlier = (
        lax.broadcasted_iota(jnp.int32, (rows, rows), 0) > lax.broadcasted_iota(jnp.int32, (rows, rows), 1)
    ).astype(jnp.bfloat16)
    counts = jnp.dot(earlier, member, preferred_element_type=jnp.float32)
    position = jnp.sum(counts * member.astype(jnp.float32), axis=1).astype(jnp.int32)
    target = languages % lang_count * (per_owner * CAP) + languages // lang_count * CAP + position
    slots = lax.broadcasted_iota(jnp.int32, (lang_count * per_owner * CAP, 1), 0)
    chooser = (slots == target[None, :]).astype(jnp.bfloat16)
    outgoing = jnp.dot(chooser, coords, preferred_element_type=jnp.float32).astype(jnp.bfloat16)
    return lax.all_to_all(outgoing, ("z", "core"), split_axis=0, concat_axis=0, tiled=True)


def solution(mesh):
    lang = mesh.shape["lang"]
    split = Mesh(mesh.devices.reshape(mesh.shape["sk"], lang // CORES, CORES), ("sk", "z", "core"))
    spec = P(("sk", "z", "core"), None)
    return jax.shard_map(
        on_device, mesh=split, in_specs=(spec, spec, spec), out_specs=spec, check_vma=False
    )
```
